512 devices in a mesh: replica: 32 (over x, y_hi, core), fsdp: 16 (over y_lo, z).
Axes of the slice: x: 4, y: 8 (y_hi: 4, y_lo: 2; y = y_hi * 2 + y_lo), z: 8, core: 2. Of those that a mesh axis runs over, the one named last changes fastest.
Arguments:
- numerators: float32 [32, 4096, 512], P('replica', 'fsdp'), may hold values from -6 to 6
- push_weights: float32 [32], P('replica'), may hold values from 0.5 to 2
- step_power: int32 [1], replicated, may hold values from 0 to 2
- activations: bfloat16 [32, 6144, 4096], P('replica', 'fsdp'), may hold values from -6 to 6
- targets: bfloat16 [32, 6144, 512], P('replica', 'fsdp'), may hold values from -6 to 6
- gain: float32 [4096], replicated, may hold values from 0.1 to 1.9
Outputs:
- mixed_numerators: float32 [32, 4096, 512], P('replica', 'fsdp')
- mixed_weights: float32 [32], P('replica')
The draws below stay inside these ranges and needn't reach their ends.
All inputs are finite; a program needn't handle non-finite values.
Results may differ from the reference program's by a relative error of at most 0.015.
Values may be sent and summed in bfloat16 or wider, within the bound.
No kernel may reach another device: no remote copies, remote signals or barrier semaphores. Data moves between devices by JAX's collectives and lax.ppermute only.
A program may use at most 64 MiB of HBM per device.

```python
import math
import jax
import jax.numpy as jnp
from jax import lax

D = 4096
KVW = 512
TOK_DEV = 384
DIST_KINDS = 3
REPLICAS = 32
FTOK = 6144
N_FSDP = 16


def shard_levels(stream_key, extent, split, low, high):
    loudness, own = 1.0, jax.random.fold_in(stream_key, 6)
    for position, shards_of in split:
        steps = jnp.exp(jax.random.uniform(jax.random.fold_in(own, position), (shards_of,), jnp.float32, low / len(split), high / len(split)))
        loudness = loudness * jnp.repeat(steps, extent[position] // shards_of).reshape([-1 if axis == position else 1 for axis in range(len(extent))])
    return loudness


def scatter_about(own_key, extent, deviation, reach, shards=(), dtype=jnp.bfloat16):
    drawn = deviation * jax.random.normal(own_key, extent, jnp.float32)
    if shards:
        drawn = drawn * shard_levels(own_key, extent, shards, -0.22, 0.18)
    return jnp.clip(drawn, -reach, reach).astype(dtype)


def setup_inputs(seed: int = 0) -> dict:
    arg_keys = jax.random.split(jax.random.key(seed), 7)
    numerators = scatter_about(arg_keys[0], (REPLICAS, D, KVW), 1.0, 6.0, ((0, 32), (1, 16)), jnp.float32)
    push_weights = jnp.clip(jnp.exp(math.log(2.0) - 1.3862944 * jax.random.uniform(arg_keys[1], (REPLICAS,), jnp.float32) ** shard_levels(arg_keys[1], (REPLICAS,), ((0, 32),), -0.2, 0.2)), 0.5, 2.0)
    step_power = jax.random.randint(arg_keys[2], (1,), 0, DIST_KINDS).astype(jnp.int32)
    activations = scatter_about(arg_keys[3], (REPLICAS, FTOK, D), 1.0, 6.0, ((0, 32), (1, 16)))
    targets = scatter_about(arg_keys[4], (REPLICAS, FTOK, KVW), 1.0, 6.0, ((0, 32), (1, 16)))
    gain = jnp.clip(1.0 + 0.18 * jax.random.normal(arg_keys[5], (D,), jnp.float32), 0.1, 1.9)
    return {"numerators": numerators, "push_weights": push_weights, "step_power": step_power, "activations": activations, "targets": targets, "gain": gain}


def replica_step(numer, weight, acts, tgts, gain):
    params = (numer / weight).astype(jnp.bfloat16)
    act32 = acts.astype(jnp.float32)
    mean_sq = lax.optimization_barrier(jnp.mean(act32 * act32, axis=1, keepdims=True))
    normed = (act32 * lax.rsqrt(mean_sq + 1e-05) * gain[None, :]).astype(jnp.bfloat16)
    keys = jnp.dot(normed, params, preferred_element_type=jnp.float32) / math.sqrt(D)
    errors = ((keys - tgts.astype(jnp.float32)) / math.sqrt(FTOK)).astype(jnp.bfloat16)
    blocks_n = normed.reshape(N_FSDP, TOK_DEV, D).astype(jnp.float32)
    blocks_e = errors.reshape(N_FSDP, TOK_DEV, KVW).astype(jnp.float32)
    partial_grads = jnp.einsum('ntd,ntk->ndk', blocks_n, blocks_e).astype(jnp.bfloat16)
    grad = lax.optimization_barrier(jnp.sum(partial_grads.astype(jnp.float32), axis=0))
    return numer - 0.3 * grad

def reference(numerators, push_weights, step_power, activations, targets, gain):

    def one(items):
        numer, weight, acts, tgts = items
        return replica_step(numer, weight, acts, tgts, gain)
    updated = lax.map(one, (numerators, push_weights, activations, targets))
    shift_by = jnp.left_shift(jnp.int32(1), step_power[0].astype(jnp.int32))
    peer_numer = jnp.roll(updated, shift_by, axis=0)
    peer_weight = jnp.roll(push_weights, shift_by, axis=0)
    mixed_numerators = 0.5 * (updated + peer_numer)
    mixed_weights = 0.5 * (push_weights + peer_weight)
    return (mixed_numerators, mixed_weights)
```

```python
from functools import partial
import math

import jax
import jax.numpy as jnp
from jax import lax
from jax.sharding import Mesh, PartitionSpec as P

DIST_KINDS = 3
PAIR = 2


def passed_along(value, axis, steps):
    count = lax.axis_size(axis)
    pairs = [(source, (source + steps) % count) for source in range(count)]
    return lax.ppermute(value, axis, pairs)


def send_to_peer(pair, by):
    return passed_along(pair, "replica", by)


def to_peer(sender, operand, power):
    branches = [partial(sender, by=1 << bit) for bit in range(DIST_KINDS)]
    return lax.switch(power, branches, operand)


def body(numerators, push_weights, step_power, activations, targets, gain):
    numer = numerators[0]
    power = step_power[0]
    features = activations.shape[2]
    n_pair = lax.axis_size("fl")
    n_ring = lax.axis_size("fz")
    replica_tokens = activations.shape[1] * n_pair * n_ring
    params = (numer / push_weights[0]).astype(jnp.bfloat16)
    gathered = lax.all_gather(params, "fl", axis=0)
    gathered = lax.all_gather(gathered, "fz", axis=0)
    full_params = gathered.reshape(-1, params.shape[1])
    peer_numer, peer_weight = to_peer(send_to_peer, (numer, push_weights), power)
    act32 = activations[0].astype(jnp.float32)
    mean_sq = jnp.mean(act32 * act32, axis=1, keepdims=True)
    normed = (act32 * lax.rsqrt(mean_sq + 1e-05) * gain[None, :]).astype(jnp.bfloat16)
    tokens = normed.shape[0]
    normed = normed.reshape(tokens, n_pair, n_ring, -1).transpose(0, 2, 1, 3).reshape(tokens, -1)
    keys = jnp.dot(normed, full_params, preferred_element_type=jnp.float32) / math.sqrt(features)
    errors = ((keys - targets[0].astype(jnp.float32)) / math.sqrt(replica_tokens)).astype(
        jnp.bfloat16
    )
    peer_numer, peer_weight, errors = lax.optimization_barrier((peer_numer, peer_weight, errors))
    partial_grad = lax.dot_general(
        normed, errors, (((0,), (0,)), ((), ())), preferred_element_type=jnp.float32
    ).astype(jnp.bfloat16)
    blocks = partial_grad.reshape(n_ring, n_pair, -1, partial_grad.shape[1])
    grad16 = lax.psum_scatter(blocks, "fz", scatter_dimension=0)
    grad16 = lax.psum_scatter(grad16, "fl", scatter_dimension=0)
    peer_grad16 = to_peer(send_to_peer, grad16, power)
    updated = numer - 0.3 * grad16.astype(jnp.float32)
    peer_updated = peer_numer - 0.3 * peer_grad16.astype(jnp.float32)
    mixed_numerators = 0.5 * (updated + peer_updated)
    mixed_weights = 0.5 * (push_weights + peer_weight)
    return (mixed_numerators[None], mixed_weights)


def solution(mesh):
    n_replica, n_fsdp = mesh.devices.shape
    split = Mesh(mesh.devices.reshape(n_replica, PAIR, n_fsdp // PAIR), ("replica", "fl", "fz"))
    rows = P("replica", ("fl", "fz"), None)
    return jax.shard_map(
        body,
        mesh=split,
        in_specs=(rows, P("replica"), P(), rows, rows, P()),
        out_specs=(rows, P("replica")),
        check_vma=False,
    )
```

```python
from functools import partial
import math

import jax
import jax.numpy as jnp
from jax import lax
from jax.sharding import Mesh, PartitionSpec as P

DIST_KINDS = 3
PAIR = 2


def passed_along(value, axis, steps):
    count = lax.axis_size(axis)
    pairs = [(source, (source + steps) % count) for source in range(count)]
    return lax.ppermute(value, axis, pairs)


def send_to_peer(pair, by):
    return passed_along(pair, "replica", by)


def finish_and_send(halves, by):
    mine, other = halves
    n_replica = lax.axis_size("replica")
    n_pair = lax.axis_size("fl")
    flip = [(side, n_pair - 1 - side) for side in range(n_pair)]
    diagonal = [
        (r * n_pair + side, ((r + by) % n_replica) * n_pair + n_pair - 1 - side)
        for r in range(n_replica)
        for side in range(n_pair)
    ]
    from_partner = lax.ppermute(other, "fl", flip)
    peer_mine = passed_along(mine, "replica", by)
    peer_other = lax.ppermute(other, ("replica", "fl"), diagonal)
    return from_partner, peer_mine, peer_other


def to_peer(sender, operand, power):
    branches = [partial(sender, by=1 << bit) for bit in range(DIST_KINDS)]
    return lax.switch(power, branches, operand)


def body(numerators, push_weights, step_power, activations, targets, gain):
    numer = numerators[0]
    power = step_power[0]
    features = activations.shape[2]
    n_pair = lax.axis_size("fl")
    n_ring = lax.axis_size("fz")
    replica_tokens = activations.shape[1] * n_pair * n_ring
    params = (numer / push_weights[0]).astype(jnp.bfloat16)
    gathered = lax.all_gather(params, "fl", axis=0)
    gathered = lax.all_gather(gathered, "fz", axis=0)
    full_params = gathered.reshape(-1, params.shape[1])
    peer_numer, peer_weight = to_peer(send_to_peer, (numer, push_weights), power)
    act32 = activations[0].astype(jnp.float32)
    mean_sq = jnp.mean(act32 * act32, axis=1, keepdims=True)
    normed = (act32 * lax.rsqrt(mean_sq + 1e-05) * gain[None, :]).astype(jnp.bfloat16)
    tokens = normed.shape[0]
    normed = normed.reshape(tokens, n_pair, n_ring, -1).transpose(0, 2, 1, 3).reshape(tokens, -1)
    keys = jnp.dot(normed, full_params, preferred_element_type=jnp.float32) / math.sqrt(features)
    errors = ((keys - targets[0].astype(jnp.float32)) / math.sqrt(replica_tokens)).astype(
        jnp.bfloat16
    )
    peer_numer, peer_weight, errors = lax.optimization_barrier((peer_numer, peer_weight, errors))
    partial_grad = lax.dot_general(
        normed, errors, (((0,), (0,)), ((), ())), preferred_element_type=jnp.float32
    ).astype(jnp.bfloat16)
    blocks = partial_grad.reshape(n_ring, n_pair, -1, partial_grad.shape[1])
    halves = lax.psum_scatter(blocks, "fz", scatter_dimension=0)
    side = lax.axis_index("fl")
    mine = lax.dynamic_index_in_dim(halves, side, 0, keepdims=False)
    other = lax.dynamic_index_in_dim(halves, n_pair - 1 - side, 0, keepdims=False)
    from_partner, peer_mine, peer_other = to_peer(finish_and_send, (mine, other), power)
    grad = mine.astype(jnp.float32) + from_partner.astype(jnp.float32)
    peer_grad = peer_mine.astype(jnp.float32) + peer_other.astype(jnp.float32)
    updated = numer - 0.3 * grad
    peer_updated = peer_numer - 0.3 * peer_grad
    mixed_numerators = 0.5 * (updated + peer_updated)
    mixed_weights = 0.5 * (push_weights + peer_weight)
    return (mixed_numerators[None], mixed_weights)


def solution(mesh):
    n_replica, n_fsdp = mesh.devices.shape
    split = Mesh(mesh.devices.reshape(n_replica, PAIR, n_fsdp // PAIR), ("replica", "fl", "fz"))
    rows = P("replica", ("fl", "fz"), None)
    return jax.shard_map(
        body,
        mesh=split,
        in_specs=(rows, P("replica"), P(), rows, rows, P()),
        out_specs=(rows, P("replica")),
        check_vma=False,
    )
```

```python
from functools import partial
import math

import jax
import jax.numpy as jnp
from jax import lax
from jax.sharding import Mesh, PartitionSpec as P

DIST_KINDS = 3
PAIR = 2


def passed_along(value, axis, steps):
    count = lax.axis_size(axis)
    pairs = [(source, (source + steps) % count) for source in range(count)]
    return lax.ppermute(value, axis, pairs)


def send_to_peer(pair, by):
    return passed_along(pair, "replica", by)


def finish_and_send(halves, by):
    mine, other = halves
    n_replica = lax.axis_size("replica")
    n_pair = lax.axis_size("fl")
    flip = [(side, n_pair - 1 - side) for side in range(n_pair)]
    diagonal = [
        (r * n_pair + side, ((r + by) % n_replica) * n_pair + n_pair - 1 - side)
        for r in range(n_replica)
        for side in range(n_pair)
    ]
    from_partner = lax.ppermute(other, "fl", flip)
    peer_mine = passed_along(mine, "replica", by)
    peer_other = lax.ppermute(other, ("replica", "fl"), diagonal)
    return from_partner, peer_mine, peer_other


def ring_gather(block):
    n = lax.axis_size("fz")
    forward = [(i, (i + 1) % n) for i in range(n)]
    backward = [(i, (i - 1) % n) for i in range(n)]
    by_offset = {0: block}
    ahead = behind = block
    for k in range(1, n // 2 + 1):
        ahead = lax.ppermute(ahead, "fz", forward)
        by_offset[(n - k) % n] = ahead
    for k in range(1, (n - 1) // 2 + 1):
        behind = lax.ppermute(behind, "fz", backward)
        by_offset[k] = behind
    stacked = jnp.stack([by_offset[o] for o in range(n)])
    doubled = jnp.concatenate([stacked, stacked])
    start = (n - lax.axis_index("fz")) % n
    return lax.dynamic_slice_in_dim(doubled, start, n, axis=0)


def gather_and_send(operand, by):
    numer, weight, block = operand
    return passed_along((numer, weight), "replica", by), ring_gather(block)


def to_peer(sender, operand, power):
    branches = [partial(sender, by=1 << bit) for bit in range(DIST_KINDS)]
    return lax.switch(power, branches, operand)


def body(numerators, push_weights, step_power, activations, targets, gain):
    numer = numerators[0]
    power = step_power[0]
    features = activations.shape[2]
    n_pair = lax.axis_size("fl")
    n_ring = lax.axis_size("fz")
    replica_tokens = activations.shape[1] * n_pair * n_ring
    params = (numer / push_weights[0]).astype(jnp.bfloat16)
    gathered = lax.all_gather(params, "fl", axis=0)
    half = gathered.shape[-1] // 2
    on_sparse = lax.all_gather(gathered[..., :half], "fz", axis=0)
    (peer_numer, peer_weight), on_ring = to_peer(
        gather_and_send, (numer, push_weights, gathered[..., half:]), power
    )
    full_params = jnp.concatenate([on_sparse, on_ring], axis=-1).reshape(-1, params.shape[1])
    act32 = activations[0].astype(jnp.float32)
    mean_sq = jnp.mean(act32 * act32, axis=1, keepdims=True)
    normed = (act32 * lax.rsqrt(mean_sq + 1e-05) * gain[None, :]).astype(jnp.bfloat16)
    tokens = normed.shape[0]
    normed = normed.reshape(tokens, n_pair, n_ring, -1).transpose(0, 2, 1, 3).reshape(tokens, -1)
    keys = jnp.dot(normed, full_params, preferred_element_type=jnp.float32) / math.sqrt(features)
    errors = ((keys - targets[0].astype(jnp.float32)) / math.sqrt(replica_tokens)).astype(
        jnp.bfloat16
    )
    partial_grad = lax.dot_general(
        normed, errors, (((0,), (0,)), ((), ())), preferred_element_type=jnp.float32
    ).astype(jnp.bfloat16)
    blocks = partial_grad.reshape(n_ring, n_pair, -1, partial_grad.shape[1])
    halves = lax.psum_scatter(blocks, "fz", scatter_dimension=0)
    side = lax.axis_index("fl")
    mine = lax.dynamic_index_in_dim(halves, side, 0, keepdims=False)
    other = lax.dynamic_index_in_dim(halves, n_pair - 1 - side, 0, keepdims=False)
    from_partner, peer_mine, peer_other = to_peer(finish_and_send, (mine, other), power)
    grad = mine.astype(jnp.float32) + from_partner.astype(jnp.float32)
    peer_grad = peer_mine.astype(jnp.float32) + peer_other.astype(jnp.float32)
    updated = numer - 0.3 * grad
    peer_updated = peer_numer - 0.3 * peer_grad
    mixed_numerators = 0.5 * (updated + peer_updated)
    mixed_weights = 0.5 * (push_weights + peer_weight)
    return (mixed_numerators[None], mixed_weights)


def solution(mesh):
    n_replica, n_fsdp = mesh.devices.shape
    split = Mesh(mesh.devices.reshape(n_replica, PAIR, n_fsdp // PAIR), ("replica", "fl", "fz"))
    rows = P("replica", ("fl", "fz"), None)
    return jax.shard_map(
        body,
        mesh=split,
        in_specs=(rows, P("replica"), P(), rows, rows, P()),
        out_specs=(rows, P("replica")),
        check_vma=False,
    )
```

```python
from functools import partial
import math

import jax
import jax.numpy as jnp
from jax import lax
from jax.sharding import Mesh, PartitionSpec as P

DIST_KINDS = 3
PAIR = 2


def passed_along(value, axis, steps):
    count = lax.axis_size(axis)
    pairs = [(source, (source + steps) % count) for source in range(count)]
    return lax.ppermute(value, axis, pairs)


def send_to_peer(pair, by):
    return passed_along(pair, "replica", by)


def finish_and_send(halves, by):
    mine, other = halves
    n_replica = lax.axis_size("replica")
    n_pair = lax.axis_size("fl")
    flip = [(side, n_pair - 1 - side) for side in range(n_pair)]
    diagonal = [
        (r * n_pair + side, ((r + by) % n_replica) * n_pair + n_pair - 1 - side)
        for r in range(n_replica)
        for side in range(n_pair)
    ]
    from_partner = lax.ppermute(other, "fl", flip)
    peer_mine = passed_along(mine, "replica", by)
    peer_other = lax.ppermute(other, ("replica", "fl"), diagonal)
    return from_partner, peer_mine, peer_other


def ring_blocks(block):
    n = lax.axis_size("fz")
    forward = [(i, (i + 1) % n) for i in range(n)]
    backward = [(i, (i - 1) % n) for i in range(n)]
    by_offset = {0: block}
    ahead = behind = block
    for k in range(1, n // 2 + 1):
        ahead = lax.ppermute(ahead, "fz", forward)
        by_offset[(n - k) % n] = ahead
    for k in range(1, (n - 1) // 2 + 1):
        behind = lax.ppermute(behind, "fz", backward)
        by_offset[k] = behind
    return by_offset


def to_peer(sender, operand, power):
    branches = [partial(sender, by=1 << bit) for bit in range(DIST_KINDS)]
    return lax.switch(power, branches, operand)


def body(numerators, push_weights, step_power, activations, targets, gain):
    numer = numerators[0]
    power = step_power[0]
    features = activations.shape[2]
    n_pair = lax.axis_size("fl")
    n_ring = lax.axis_size("fz")
    replica_tokens = activations.shape[1] * n_pair * n_ring
    params = (numer / push_weights[0]).astype(jnp.bfloat16)
    side = lax.axis_index("fl")
    spot = lax.axis_index("fz")
    own_row = lax.all_gather(params, "fz", axis=0, tiled=True)
    flip = [(i, n_pair - 1 - i) for i in range(n_pair)]
    partner_rows = ring_blocks(lax.ppermute(params, "fl", flip))
    act32 = activations[0].astype(jnp.float32)
    mean_sq = jnp.mean(act32 * act32, axis=1, keepdims=True)
    normed = (act32 * lax.rsqrt(mean_sq + 1e-05) * gain[None, :]).astype(jnp.bfloat16)
    tokens = normed.shape[0]
    normed = normed.reshape(tokens, n_pair, n_ring, -1).transpose(0, 2, 1, 3).reshape(tokens, -1)
    by_block = normed.reshape(tokens, n_ring, n_pair, -1)
    own_cols = lax.dynamic_index_in_dim(by_block, side, 2, keepdims=False).reshape(tokens, -1)
    keys = jnp.dot(own_cols, own_row, preferred_element_type=jnp.float32)
    for offset, rows in sorted(partner_rows.items()):
        cols = lax.dynamic_slice(
            by_block, (0, (spot + offset) % n_ring, n_pair - 1 - side, 0), (tokens, 1, 1, rows.shape[0])
        ).reshape(tokens, -1)
        keys = keys + jnp.dot(cols, rows, preferred_element_type=jnp.float32)
    keys = keys / math.sqrt(features)
    errors = ((keys - targets[0].astype(jnp.float32)) / math.sqrt(replica_tokens)).astype(
        jnp.bfloat16
    )
    partial_grad = lax.dot_general(
        normed, errors, (((0,), (0,)), ((), ())), preferred_element_type=jnp.float32
    ).astype(jnp.bfloat16)
    early, weight, partial_grad = lax.optimization_barrier((numer, push_weights, partial_grad))
    peer_numer, peer_weight = to_peer(send_to_peer, (early, weight), power)
    blocks = partial_grad.reshape(n_ring, n_pair, -1, partial_grad.shape[1])
    halves = lax.psum_scatter(blocks, "fz", scatter_dimension=0)
    mine = lax.dynamic_index_in_dim(halves, side, 0, keepdims=False)
    other = lax.dynamic_index_in_dim(halves, n_pair - 1 - side, 0, keepdims=False)
    from_partner, peer_mine, peer_other = to_peer(finish_and_send, (mine, other), power)
    grad = mine.astype(jnp.float32) + from_partner.astype(jnp.float32)
    peer_grad = peer_mine.astype(jnp.float32) + peer_other.astype(jnp.float32)
    updated = numer - 0.3 * grad
    peer_updated = peer_numer - 0.3 * peer_grad
    mixed_numerators = 0.5 * (updated + peer_updated)
    mixed_weights = 0.5 * (push_weights + peer_weight)
    return (mixed_numerators[None], mixed_weights)


def solution(mesh):
    n_replica, n_fsdp = mesh.devices.shape
    split = Mesh(mesh.devices.reshape(n_replica, PAIR, n_fsdp // PAIR), ("replica", "fl", "fz"))
    rows = P("replica", ("fl", "fz"), None)
    return jax.shard_map(
        body,
        mesh=split,
        in_specs=(rows, P("replica"), P(), rows, rows, P()),
        out_specs=(rows, P("replica")),
        check_vma=False,
    )
```

```python
from functools import partial
import math

import jax
import jax.numpy as jnp
from jax import lax
from jax.sharding import Mesh, PartitionSpec as P

DIST_KINDS = 3
PAIR = 2


def passed_along(value, axis, steps):
    count = lax.axis_size(axis)
    pairs = [(source, (source + steps) % count) for source in range(count)]
    return lax.ppermute(value, axis, pairs)


def send_to_peer(pair, by):
    return passed_along(pair, "replica", by)


def to_peer(sender, operand, power):
    branches = [partial(sender, by=1 << bit) for bit in range(DIST_KINDS)]
    return lax.switch(power, branches, operand)


def body(numerators, push_weights, step_power, activations, targets, gain):
    numer = numerators[0]
    power = step_power[0]
    features = activations.shape[2]
    n_pair = lax.axis_size("fl")
    n_ring = lax.axis_size("fz")
    replica_tokens = activations.shape[1] * n_pair * n_ring
    params = (numer / push_weights[0]).astype(jnp.bfloat16)
    gathered = lax.all_gather(params, "fl", axis=0)
    gathered = lax.all_gather(gathered, "fz", axis=0)
    full_params = gathered.reshape(-1, params.shape[1])
    peer_numer, peer_weight = to_peer(send_to_peer, (numer, push_weights), power)
    act32 = activations[0].astype(jnp.float32)
    mean_sq = jnp.mean(act32 * act32, axis=1, keepdims=True)
    normed = (act32 * lax.rsqrt(mean_sq + 1e-05) * gain[None, :]).astype(jnp.bfloat16)
    tokens = normed.shape[0]
    normed = normed.reshape(tokens, n_pair, n_ring, -1).transpose(0, 2, 1, 3).reshape(tokens, -1)
    keys = jnp.dot(normed, full_params, preferred_element_type=jnp.float32) / math.sqrt(features)
    errors = ((keys - targets[0].astype(jnp.float32)) / math.sqrt(replica_tokens)).astype(
        jnp.bfloat16
    )
    peer_numer, peer_weight, errors = lax.optimization_barrier((peer_numer, peer_weight, errors))
    partial_grad = lax.dot_general(
        normed, errors, (((0,), (0,)), ((), ())), preferred_element_type=jnp.float32
    ).astype(jnp.bfloat16)
    blocks = partial_grad.reshape(n_ring, n_pair, -1, partial_grad.shape[1])
    halves = lax.psum_scatter(blocks, "fz", scatter_dimension=0)
    side = lax.axis_index("fl")
    mine = lax.dynamic_index_in_dim(halves, side, 0, keepdims=False)
    other = lax.dynamic_index_in_dim(halves, n_pair - 1 - side, 0, keepdims=False)
    flip = [(i, n_pair - 1 - i) for i in range(n_pair)]
    from_partner = lax.ppermute(other, "fl", flip)
    grad = mine.astype(jnp.float32) + from_partner.astype(jnp.float32)
    peer_grad = to_peer(send_to_peer, grad.astype(jnp.bfloat16), power).astype(jnp.float32)
    updated = numer - 0.3 * grad
    peer_updated = peer_numer - 0.3 * peer_grad
    mixed_numerators = 0.5 * (updated + peer_updated)
    mixed_weights = 0.5 * (push_weights + peer_weight)
    return (mixed_numerators[None], mixed_weights)


def solution(mesh):
    n_replica, n_fsdp = mesh.devices.shape
    split = Mesh(mesh.devices.reshape(n_replica, PAIR, n_fsdp // PAIR), ("replica", "fl", "fz"))
    rows = P("replica", ("fl", "fz"), None)
    return jax.shard_map(
        body,
        mesh=split,
        in_specs=(rows, P("replica"), P(), rows, rows, P()),
        out_specs=(rows, P("replica")),
        check_vma=False,
    )
```

```python
from functools import partial
import math

import jax
import jax.numpy as jnp
from jax import lax
from jax.experimental import pallas as pl
from jax.experimental.pallas import tpu as pltpu
from jax.sharding import Mesh, PartitionSpec as P

DIST_KINDS = 3
PAIR = 2
CHUNK = 512


def grad_kernel(normed_ref, normed_t_ref, params_ref, targets_ref, out_ref, keys_acc, errors_ref, *, key_scale, error_scale):
    keys_acc[...] = jnp.zeros_like(keys_acc)

    def key_step(i, carry):
        at = pl.multiple_of(i * CHUNK, CHUNK)
        keys_acc[...] += jnp.dot(
            normed_ref[:, pl.ds(at, CHUNK)], params_ref[pl.ds(at, CHUNK), :],
            preferred_element_type=jnp.float32,
        )
        return carry

    lax.fori_loop(0, normed_ref.shape[1] // CHUNK, key_step, 0)
    keys = keys_acc[...] / key_scale
    errors_ref[...] = ((keys - targets_ref[...].astype(jnp.float32)) / error_scale).astype(jnp.bfloat16)

    def grad_step(i, carry):
        at = pl.multiple_of(i * CHUNK, CHUNK)
        out_ref[pl.ds(at, CHUNK), :] = jnp.dot(
            normed_t_ref[pl.ds(at, CHUNK), :], errors_ref[...],
            preferred_element_type=jnp.float32,
        ).astype(jnp.bfloat16)
        return carry

    lax.fori_loop(0, normed_t_ref.shape[0] // CHUNK, grad_step, 0)


def block_gradient(normed, params, targets, key_scale, error_scale):
    tokens, features = normed.shape
    width = params.shape[1]
    flops = 4 * tokens * features * width
    moved = 2 * (2 * tokens * features + 2 * features * width + tokens * width)
    vmem = pl.BlockSpec(memory_space=pltpu.VMEM)
    return pl.pallas_call(
        partial(grad_kernel, key_scale=key_scale, error_scale=error_scale),
        out_shape=jax.ShapeDtypeStruct((features, width), jnp.bfloat16),
        in_specs=[vmem] * 4,
        out_specs=vmem,
        scratch_shapes=[pltpu.VMEM((tokens, width), jnp.float32), pltpu.VMEM((tokens, width), jnp.bfloat16)],
        cost_estimate=pl.CostEstimate(flops=flops, bytes_accessed=moved, transcendentals=0),
    )(normed, normed.T, params, targets)


def passed_along(value, axis, steps):
    count = lax.axis_size(axis)
    pairs = [(source, (source + steps) % count) for source in range(count)]
    return lax.ppermute(value, axis, pairs)


def send_to_peer(pair, by):
    return passed_along(pair, "replica", by)


def finish_and_send(halves, by):
    mine, other = halves
    n_replica = lax.axis_size("replica")
    n_pair = lax.axis_size("fl")
    flip = [(side, n_pair - 1 - side) for side in range(n_pair)]
    diagonal = [
        (r * n_pair + side, ((r + by) % n_replica) * n_pair + n_pair - 1 - side)
        for r in range(n_replica)
        for side in range(n_pair)
    ]
    from_partner = lax.ppermute(other, "fl", flip)
    peer_mine = passed_along(mine, "replica", by)
    peer_other = lax.ppermute(other, ("replica", "fl"), diagonal)
    return from_partner, peer_mine, peer_other


def to_peer(sender, operand, power):
    branches = [partial(sender, by=1 << bit) for bit in range(DIST_KINDS)]
    return lax.switch(power, branches, operand)


def body(numerators, push_weights, step_power, activations, targets, gain):
    numer = numerators[0]
    power = step_power[0]
    features = activations.shape[2]
    n_pair = lax.axis_size("fl")
    n_ring = lax.axis_size("fz")
    replica_tokens = activations.shape[1] * n_pair * n_ring
    params = (numer / push_weights[0]).astype(jnp.bfloat16)
    gathered = lax.all_gather(params, "fl", axis=0)
    gathered = lax.all_gather(gathered, "fz", axis=0)
    full_params = gathered.reshape(-1, params.shape[1])
    peer_numer, peer_weight = to_peer(send_to_peer, (numer, push_weights), power)
    act32 = activations[0].astype(jnp.float32)
    mean_sq = jnp.mean(act32 * act32, axis=1, keepdims=True)
    normed = (act32 * lax.rsqrt(mean_sq + 1e-05) * gain[None, :]).astype(jnp.bfloat16)
    tokens = normed.shape[0]
    normed = normed.reshape(tokens, n_pair, n_ring, -1).transpose(0, 2, 1, 3).reshape(tokens, -1)
    peer_numer, peer_weight, normed = lax.optimization_barrier((peer_numer, peer_weight, normed))
    partial_grad = block_gradient(
        normed, full_params, targets[0], math.sqrt(features), math.sqrt(replica_tokens)
    )
    blocks = partial_grad.reshape(n_ring, n_pair, -1, partial_grad.shape[1])
    halves = lax.psum_scatter(blocks, "fz", scatter_dimension=0)
    side = lax.axis_index("fl")
    mine = lax.dynamic_index_in_dim(halves, side, 0, keepdims=False)
    other = lax.dynamic_index_in_dim(halves, n_pair - 1 - side, 0, keepdims=False)
    from_partner, peer_mine, peer_other = to_peer(finish_and_send, (mine, other), power)
    grad = mine.astype(jnp.float32) + from_partner.astype(jnp.float32)
    peer_grad = peer_mine.astype(jnp.float32) + peer_other.astype(jnp.float32)
    updated = numer - 0.3 * grad
    peer_updated = peer_numer - 0.3 * peer_grad
    mixed_numerators = 0.5 * (updated + peer_updated)
    mixed_weights = 0.5 * (push_weights + peer_weight)
    return (mixed_numerators[None], mixed_weights)


def solution(mesh):
    n_replica, n_fsdp = mesh.devices.shape
    split = Mesh(mesh.devices.reshape(n_replica, PAIR, n_fsdp // PAIR), ("replica", "fl", "fz"))
    rows = P("replica", ("fl", "fz"), None)
    return jax.shard_map(
        body,
        mesh=split,
        in_specs=(rows, P("replica"), P(), rows, rows, P()),
        out_specs=(rows, P("replica")),
        check_vma=False,
    )
```

```python
from functools import partial
import math

import jax
import jax.numpy as jnp
from jax import lax
from jax.sharding import Mesh, PartitionSpec as P

DIST_KINDS = 3
PAIR = 2


def passed_along(value, axis, steps):
    count = lax.axis_size(axis)
    pairs = [(source, (source + steps) % count) for source in range(count)]
    return lax.ppermute(value, axis, pairs)


def send_to_peer(pair, by):
    return passed_along(pair, "replica", by)


def to_peer(sender, operand, power):
    branches = [partial(sender, by=1 << bit) for bit in range(DIST_KINDS)]
    return lax.switch(power, branches, operand)


def body(numerators, push_weights, step_power, activations, targets, gain):
    numer = numerators[0]
    power = step_power[0]
    features = activations.shape[2]
    n_pair = lax.axis_size("fl")
    n_ring = lax.axis_size("fz")
    replica_tokens = activations.shape[1] * n_pair * n_ring
    params = (numer / push_weights[0]).astype(jnp.bfloat16)
    gathered = lax.all_gather(params, "fl", axis=0)
    gathered = lax.all_gather(gathered, "fz", axis=0)
    full_params = gathered.reshape(-1, params.shape[1])
    peer_numer, peer_weight = to_peer(send_to_peer, (numer, push_weights), power)
    act32 = activations[0].astype(jnp.float32)
    mean_sq = jnp.mean(act32 * act32, axis=1, keepdims=True)
    normed = (act32 * lax.rsqrt(mean_sq + 1e-05) * gain[None, :]).astype(jnp.bfloat16)
    tokens = normed.shape[0]
    normed = normed.reshape(tokens, n_pair, n_ring, -1).transpose(0, 2, 1, 3).reshape(tokens, -1)
    keys = jnp.dot(normed, full_params, preferred_element_type=jnp.float32) / math.sqrt(features)
    errors = ((keys - targets[0].astype(jnp.float32)) / math.sqrt(replica_tokens)).astype(
        jnp.bfloat16
    )
    peer_numer, peer_weight, errors = lax.optimization_barrier((peer_numer, peer_weight, errors))
    side = lax.axis_index("fl")
    flip = [(i, n_pair - 1 - i) for i in range(n_pair)]
    by_block = normed.reshape(tokens, n_ring, n_pair, -1)
    own_cols = lax.dynamic_index_in_dim(by_block, side, 2, keepdims=False).reshape(tokens, -1)
    partner_cols = lax.dynamic_index_in_dim(by_block, n_pair - 1 - side, 2, keepdims=False)
    their_cols = lax.ppermute(partner_cols, "fl", flip).reshape(tokens, -1)
    their_errors = lax.ppermute(errors, "fl", flip)
    contract = (((0,), (0,)), ((), ()))
    mine = lax.dot_general(own_cols, errors, contract, preferred_element_type=jnp.float32)
    theirs = lax.dot_general(their_cols, their_errors, contract, preferred_element_type=jnp.float32)
    pair_sum = mine.astype(jnp.bfloat16).astype(jnp.float32) + theirs.astype(jnp.bfloat16).astype(jnp.float32)
    blocks = pair_sum.astype(jnp.bfloat16).reshape(n_ring, -1, pair_sum.shape[1])
    grad16 = lax.psum_scatter(blocks, "fz", scatter_dimension=0)
    peer_grad16 = to_peer(send_to_peer, grad16, power)
    updated = numer - 0.3 * grad16.astype(jnp.float32)
    peer_updated = peer_numer - 0.3 * peer_grad16.astype(jnp.float32)
    mixed_numerators = 0.5 * (updated + peer_updated)
    mixed_weights = 0.5 * (push_weights + peer_weight)
    return (mixed_numerators[None], mixed_weights)


def solution(mesh):
    n_replica, n_fsdp = mesh.devices.shape
    split = Mesh(mesh.devices.reshape(n_replica, PAIR, n_fsdp // PAIR), ("replica", "fl", "fz"))
    rows = P("replica", ("fl", "fz"), None)
    return jax.shard_map(
        body,
        mesh=split,
        in_specs=(rows, P("replica"), P(), rows, rows, P()),
        out_specs=(rows, P("replica")),
        check_vma=False,
    )
```

```python
from functools import partial
import math

import jax
import jax.numpy as jnp
from jax import lax
from jax.sharding import Mesh, PartitionSpec as P

DIST_KINDS = 3
PAIR = 2


def passed_along(value, axis, steps):
    count = lax.axis_size(axis)
    pairs = [(source, (source + steps) % count) for source in range(count)]
    return lax.ppermute(value, axis, pairs)


def send_to_peer(pair, by):
    return passed_along(pair, "replica", by)


def to_peer(sender, operand, power):
    branches = [partial(sender, by=1 << bit) for bit in range(DIST_KINDS)]
    return lax.switch(power, branches, operand)


def body(numerators, push_weights, step_power, activations, targets, gain):
    numer = numerators[0]
    power = step_power[0]
    features = activations.shape[2]
    n_pair = lax.axis_size("fl")
    n_ring = lax.axis_size("fz")
    replica_tokens = activations.shape[1] * n_pair * n_ring
    params = (numer / push_weights[0]).astype(jnp.bfloat16)
    gathered = lax.all_gather(params, "fl", axis=0)
    gathered = lax.all_gather(gathered, "fz", axis=0)
    full_params = gathered.reshape(-1, params.shape[1])
    act32 = activations[0].astype(jnp.float32)
    mean_sq = jnp.mean(act32 * act32, axis=1, keepdims=True)
    normed = (act32 * lax.rsqrt(mean_sq + 1e-05) * gain[None, :]).astype(jnp.bfloat16)
    tokens = normed.shape[0]
    normed = normed.reshape(tokens, n_pair, n_ring, -1).transpose(0, 2, 1, 3).reshape(tokens, -1)
    keys = jnp.dot(normed, full_params, preferred_element_type=jnp.float32) / math.sqrt(features)
    errors = ((keys - targets[0].astype(jnp.float32)) / math.sqrt(replica_tokens)).astype(
        jnp.bfloat16
    )
    side = lax.axis_index("fl")
    flip = [(i, n_pair - 1 - i) for i in range(n_pair)]
    by_block = normed.reshape(tokens, n_ring, n_pair, -1)
    own_cols = lax.dynamic_index_in_dim(by_block, side, 2, keepdims=False).reshape(tokens, -1)
    partner_cols = lax.dynamic_index_in_dim(by_block, n_pair - 1 - side, 2, keepdims=False)
    their_cols = lax.ppermute(partner_cols, "fl", flip).reshape(tokens, -1)
    their_errors = lax.ppermute(errors, "fl", flip)
    contract = (((0,), (0,)), ((), ()))
    mine = lax.dot_general(own_cols, errors, contract, preferred_element_type=jnp.float32)
    theirs = lax.dot_general(their_cols, their_errors, contract, preferred_element_type=jnp.float32)
    pair_sum = mine.astype(jnp.bfloat16).astype(jnp.float32) + theirs.astype(jnp.bfloat16).astype(jnp.float32)
    blocks = pair_sum.astype(jnp.bfloat16).reshape(n_ring, -1, pair_sum.shape[1])
    early, weight, blocks = lax.optimization_barrier((numer, push_weights, blocks))
    peer_numer, peer_weight = to_peer(send_to_peer, (early, weight), power)
    grad16 = lax.psum_scatter(blocks, "fz", scatter_dimension=0)
    peer_grad16 = to_peer(send_to_peer, grad16, power)
    updated = numer - 0.3 * grad16.astype(jnp.float32)
    peer_updated = peer_numer - 0.3 * peer_grad16.astype(jnp.float32)
    mixed_numerators = 0.5 * (updated + peer_updated)
    mixed_weights = 0.5 * (push_weights + peer_weight)
    return (mixed_numerators[None], mixed_weights)


def solution(mesh):
    n_replica, n_fsdp = mesh.devices.shape
    split = Mesh(mesh.devices.reshape(n_replica, PAIR, n_fsdp // PAIR), ("replica", "fl", "fz"))
    rows = P("replica", ("fl", "fz"), None)
    return jax.shard_map(
        body,
        mesh=split,
        in_specs=(rows, P("replica"), P(), rows, rows, P()),
        out_specs=(rows, P("replica")),
        check_vma=False,
    )
```

```python
from functools import partial
import math

import jax
import jax.numpy as jnp
from jax import lax
from jax.sharding import Mesh, PartitionSpec as P

DIST_KINDS = 3
PAIR = 2


def passed_along(value, axis, steps):
    count = lax.axis_size(axis)
    pairs = [(source, (source + steps) % count) for source in range(count)]
    return lax.ppermute(value, axis, pairs)


def send_to_peer(pair, by):
    return passed_along(pair, "replica", by)


def to_peer(sender, operand, power):
    branches = [partial(sender, by=1 << bit) for bit in range(DIST_KINDS)]
    return lax.switch(power, branches, operand)


def body(numerators, push_weights, step_power, activations, targets, gain):
    numer = numerators[0]
    power = step_power[0]
    features = activations.shape[2]
    n_pair = lax.axis_size("fl")
    n_ring = lax.axis_size("fz")
    replica_tokens = activations.shape[1] * n_pair * n_ring
    params = (numer / push_weights[0]).astype(jnp.bfloat16)
    gathered = lax.all_gather(params, "fl", axis=0)
    gathered = lax.all_gather(gathered, "fz", axis=1)
    full_params = gathered.reshape(-1, params.shape[1])
    act32 = activations[0].astype(jnp.float32)
    mean_sq = jnp.mean(act32 * act32, axis=1, keepdims=True)
    normed = (act32 * lax.rsqrt(mean_sq + 1e-05) * gain[None, :]).astype(jnp.bfloat16)
    tokens = normed.shape[0]
    keys = jnp.dot(normed, full_params, preferred_element_type=jnp.float32) / math.sqrt(features)
    errors = ((keys - targets[0].astype(jnp.float32)) / math.sqrt(replica_tokens)).astype(
        jnp.bfloat16
    )
    side = lax.axis_index("fl")
    flip = [(i, n_pair - 1 - i) for i in range(n_pair)]
    row_width = features // n_pair
    own_cols = lax.dynamic_slice_in_dim(normed, side * row_width, row_width, axis=1)
    partner_cols = lax.dynamic_slice_in_dim(normed, (n_pair - 1 - side) * row_width, row_width, axis=1)
    their_cols = lax.ppermute(partner_cols, "fl", flip)
    their_errors = lax.ppermute(errors, "fl", flip)
    contract = (((0,), (0,)), ((), ()))
    mine = lax.dot_general(own_cols, errors, contract, preferred_element_type=jnp.float32)
    theirs = lax.dot_general(their_cols, their_errors, contract, preferred_element_type=jnp.float32)
    pair_sum = mine.astype(jnp.bfloat16).astype(jnp.float32) + theirs.astype(jnp.bfloat16).astype(jnp.float32)
    blocks = pair_sum.astype(jnp.bfloat16).reshape(n_ring, -1, pair_sum.shape[1])
    early, weight, blocks = lax.optimization_barrier((numer, push_weights, blocks))
    peer_numer, peer_weight = to_peer(send_to_peer, (early, weight), power)
    grad16 = lax.psum_scatter(blocks, "fz", scatter_dimension=0)
    peer_grad16 = to_peer(send_to_peer, grad16, power)
    updated = numer - 0.3 * grad16.astype(jnp.float32)
    peer_updated = peer_numer - 0.3 * peer_grad16.astype(jnp.float32)
    mixed_numerators = 0.5 * (updated + peer_updated)
    mixed_weights = 0.5 * (push_weights + peer_weight)
    return (mixed_numerators[None], mixed_weights)


def solution(mesh):
    n_replica, n_fsdp = mesh.devices.shape
    split = Mesh(mesh.devices.reshape(n_replica, PAIR, n_fsdp // PAIR), ("replica", "fl", "fz"))
    rows = P("replica", ("fl", "fz"), None)
    return jax.shard_map(
        body,
        mesh=split,
        in_specs=(rows, P("replica"), P(), rows, rows, P()),
        out_specs=(rows, P("replica")),
        check_vma=False,
    )
```

```python
from functools import partial
import math

import jax
import jax.numpy as jnp
from jax import lax
from jax.sharding import Mesh, PartitionSpec as P

DIST_KINDS = 3
PAIR = 2


def passed_along(value, axis, steps):
    count = lax.axis_size(axis)
    pairs = [(source, (source + steps) % count) for source in range(count)]
    return lax.ppermute(value, axis, pairs)


def send_to_peer(pair, by):
    return passed_along(pair, "replica", by)


def to_peer(sender, operand, power):
    branches = [partial(sender, by=1 << bit) for bit in range(DIST_KINDS)]
    return lax.switch(power, branches, operand)


def body(numerators, push_weights, step_power, activations, targets, gain):
    numer = numerators[0]
    power = step_power[0]
    features = activations.shape[2]
    n_pair = lax.axis_size("fl")
    n_ring = lax.axis_size("fz")
    replica_tokens = activations.shape[1] * n_pair * n_ring
    params = (numer / push_weights[0]).astype(jnp.bfloat16)
    gathered = lax.all_gather(params, "fl", axis=0)
    gathered = lax.all_gather(gathered, "fz", axis=1)
    full_params = gathered.reshape(-1, params.shape[1])
    act32 = activations[0].astype(jnp.float32)
    mean_sq = jnp.mean(act32 * act32, axis=1, keepdims=True)
    normed = (act32 * lax.rsqrt(mean_sq + 1e-05) * gain[None, :]).astype(jnp.bfloat16)
    tokens = normed.shape[0]
    side = lax.axis_index("fl")
    flip = [(i, n_pair - 1 - i) for i in range(n_pair)]
    row_width = features // n_pair
    own_cols = lax.dynamic_slice_in_dim(normed, side * row_width, row_width, axis=1)
    partner_cols = lax.dynamic_slice_in_dim(normed, (n_pair - 1 - side) * row_width, row_width, axis=1)
    their_cols = lax.ppermute(partner_cols, "fl", flip)
    contract = (((0,), (0,)), ((), ()))
    half = tokens // 2
    mine = theirs = None
    for part in range(2):
        span = slice(part * half, (part + 1) * half)
        keys = jnp.dot(normed[span], full_params, preferred_element_type=jnp.float32) / math.sqrt(features)
        errors = ((keys - targets[0, span].astype(jnp.float32)) / math.sqrt(replica_tokens)).astype(
            jnp.bfloat16
        )
        their_errors = lax.ppermute(errors, "fl", flip)
        term = lax.dot_general(own_cols[span], errors, contract, preferred_element_type=jnp.float32)
        their_term = lax.dot_general(
            their_cols[span], their_errors, contract, preferred_element_type=jnp.float32
        )
        mine = term if mine is None else mine + term
        theirs = their_term if theirs is None else theirs + their_term
    pair_sum = mine.astype(jnp.bfloat16).astype(jnp.float32) + theirs.astype(jnp.bfloat16).astype(jnp.float32)
    blocks = pair_sum.astype(jnp.bfloat16).reshape(n_ring, -1, pair_sum.shape[1])
    early, weight, blocks = lax.optimization_barrier((numer, push_weights, blocks))
    peer_numer, peer_weight = to_peer(send_to_peer, (early, weight), power)
    grad16 = lax.psum_scatter(blocks, "fz", scatter_dimension=0)
    peer_grad16 = to_peer(send_to_peer, grad16, power)
    updated = numer - 0.3 * grad16.astype(jnp.float32)
    peer_updated = peer_numer - 0.3 * peer_grad16.astype(jnp.float32)
    mixed_numerators = 0.5 * (updated + peer_updated)
    mixed_weights = 0.5 * (push_weights + peer_weight)
    return (mixed_numerators[None], mixed_weights)


def solution(mesh):
    n_replica, n_fsdp = mesh.devices.shape
    split = Mesh(mesh.devices.reshape(n_replica, PAIR, n_fsdp // PAIR), ("replica", "fl", "fz"))
    rows = P("replica", ("fl", "fz"), None)
    return jax.shard_map(
        body,
        mesh=split,
        in_specs=(rows, P("replica"), P(), rows, rows, P()),
        out_specs=(rows, P("replica")),
        check_vma=False,
    )
```

```python
from functools import partial
import math

import jax
import jax.numpy as jnp
from jax import lax
from jax.sharding import Mesh, PartitionSpec as P

DIST_KINDS = 3
PAIR = 2


def passed_along(value, axis, steps):
    count = lax.axis_size(axis)
    pairs = [(source, (source + steps) % count) for source in range(count)]
    return lax.ppermute(value, axis, pairs)


def send_to_peer(pair, by):
    return passed_along(pair, "replica", by)


def to_peer(sender, operand, power):
    branches = [partial(sender, by=1 << bit) for bit in range(DIST_KINDS)]
    return lax.switch(power, branches, operand)


def body(numerators, push_weights, step_power, activations, targets, gain):
    numer = numerators[0]
    power = step_power[0]
    features = activations.shape[2]
    n_pair = lax.axis_size("fl")
    n_ring = lax.axis_size("fz")
    replica_tokens = activations.shape[1] * n_pair * n_ring
    params = (numer / push_weights[0]).astype(jnp.bfloat16)
    side = lax.axis_index("fl")
    flip = [(i, n_pair - 1 - i) for i in range(n_pair)]
    pair = jnp.stack([params, lax.ppermute(params, "fl", flip)])
    rows_by_side = lax.all_gather(pair, "fz", axis=1).reshape(n_pair, -1, params.shape[1])
    act32 = activations[0].astype(jnp.float32)
    mean_sq = jnp.mean(act32 * act32, axis=1, keepdims=True)
    normed = (act32 * lax.rsqrt(mean_sq + 1e-05) * gain[None, :]).astype(jnp.bfloat16)
    tokens = normed.shape[0]
    row_width = features // n_pair
    own_cols = lax.dynamic_slice_in_dim(normed, side * row_width, row_width, axis=1)
    partner_cols = lax.dynamic_slice_in_dim(normed, (n_pair - 1 - side) * row_width, row_width, axis=1)
    their_cols = lax.ppermute(partner_cols, "fl", flip)
    contract = (((0,), (0,)), ((), ()))
    half = tokens // 2
    mine = theirs = None
    for part in range(2):
        span = slice(part * half, (part + 1) * half)
        keys = jnp.dot(own_cols[span], rows_by_side[0], preferred_element_type=jnp.float32)
        keys = keys + jnp.dot(partner_cols[span], rows_by_side[1], preferred_element_type=jnp.float32)
        keys = keys / math.sqrt(features)
        errors = ((keys - targets[0, span].astype(jnp.float32)) / math.sqrt(replica_tokens)).astype(
            jnp.bfloat16
        )
        their_errors = lax.ppermute(errors, "fl", flip)
        term = lax.dot_general(own_cols[span], errors, contract, preferred_element_type=jnp.float32)
        their_term = lax.dot_general(
            their_cols[span], their_errors, contract, preferred_element_type=jnp.float32
        )
        mine = term if mine is None else mine + term
        theirs = their_term if theirs is None else theirs + their_term
    pair_sum = mine.astype(jnp.bfloat16).astype(jnp.float32) + theirs.astype(jnp.bfloat16).astype(jnp.float32)
    blocks = pair_sum.astype(jnp.bfloat16).reshape(n_ring, -1, pair_sum.shape[1])
    early, weight, blocks = lax.optimization_barrier((numer, push_weights, blocks))
    peer_numer, peer_weight = to_peer(send_to_peer, (early, weight), power)
    grad16 = lax.psum_scatter(blocks, "fz", scatter_dimension=0)
    peer_grad16 = to_peer(send_to_peer, grad16, power)
    updated = numer - 0.3 * grad16.astype(jnp.float32)
    peer_updated = peer_numer - 0.3 * peer_grad16.astype(jnp.float32)
    mixed_numerators = 0.5 * (updated + peer_updated)
    mixed_weights = 0.5 * (push_weights + peer_weight)
    return (mixed_numerators[None], mixed_weights)


def solution(mesh):
    n_replica, n_fsdp = mesh.devices.shape
    split = Mesh(mesh.devices.reshape(n_replica, PAIR, n_fsdp // PAIR), ("replica", "fl", "fz"))
    rows = P("replica", ("fl", "fz"), None)
    return jax.shard_map(
        body,
        mesh=split,
        in_specs=(rows, P("replica"), P(), rows, rows, P()),
        out_specs=(rows, P("replica")),
        check_vma=False,
    )
```

```python
from functools import partial
import math

import jax
import jax.numpy as jnp
from jax import lax
from jax.sharding import Mesh, PartitionSpec as P

DIST_KINDS = 3
PAIR = 2


def passed_along(value, axis, steps):
    count = lax.axis_size(axis)
    pairs = [(source, (source + steps) % count) for source in range(count)]
    return lax.ppermute(value, axis, pairs)


def send_to_peer(pair, by):
    return passed_along(pair, "replica", by)


def to_peer(sender, operand, power):
    branches = [partial(sender, by=1 << bit) for bit in range(DIST_KINDS)]
    return lax.switch(power, branches, operand)


def body(numerators, push_weights, step_power, activations, targets, gain):
    numer = numerators[0]
    power = step_power[0]
    features = activations.shape[2]
    n_pair = lax.axis_size("fl")
    n_ring = lax.axis_size("fz")
    replica_tokens = activations.shape[1] * n_pair * n_ring
    params = (numer / push_weights[0]).astype(jnp.bfloat16)
    gathered = lax.all_gather(params, "fl", axis=0)
    gathered = lax.all_gather(gathered, "fz", axis=1)
    full_params = gathered.reshape(-1, params.shape[1])
    act32 = activations[0].astype(jnp.float32)
    mean_sq = jnp.mean(act32 * act32, axis=1, keepdims=True)
    normed = (act32 * lax.rsqrt(mean_sq + 1e-05) * gain[None, :]).astype(jnp.bfloat16)
    tokens = normed.shape[0]
    side = lax.axis_index("fl")
    flip = [(i, n_pair - 1 - i) for i in range(n_pair)]
    row_width = features // n_pair
    own_cols = lax.dynamic_slice_in_dim(normed, side * row_width, row_width, axis=1)
    partner_cols = lax.dynamic_slice_in_dim(normed, (n_pair - 1 - side) * row_width, row_width, axis=1)
    their_cols = lax.ppermute(partner_cols, "fl", flip)
    contract = (((0,), (0,)), ((), ()))
    width = full_params.shape[1] // 2
    sums = []
    for part in range(2):
        span = slice(part * width, (part + 1) * width)
        keys = jnp.dot(normed, full_params[:, span], preferred_element_type=jnp.float32) / math.sqrt(features)
        errors = ((keys - targets[0][:, span].astype(jnp.float32)) / math.sqrt(replica_tokens)).astype(
            jnp.bfloat16
        )
        their_errors = lax.ppermute(errors, "fl", flip)
        mine = lax.dot_general(own_cols, errors, contract, preferred_element_type=jnp.float32)
        theirs = lax.dot_general(their_cols, their_errors, contract, preferred_element_type=jnp.float32)
        sums.append(
            mine.astype(jnp.bfloat16).astype(jnp.float32) + theirs.astype(jnp.bfloat16).astype(jnp.float32)
        )
    pair_sum = jnp.concatenate(sums, axis=1)
    blocks = pair_sum.astype(jnp.bfloat16).reshape(n_ring, -1, pair_sum.shape[1])
    early, weight, blocks = lax.optimization_barrier((numer, push_weights, blocks))
    peer_numer, peer_weight = to_peer(send_to_peer, (early, weight), power)
    grad16 = lax.psum_scatter(blocks, "fz", scatter_dimension=0)
    peer_grad16 = to_peer(send_to_peer, grad16, power)
    updated = numer - 0.3 * grad16.astype(jnp.float32)
    peer_updated = peer_numer - 0.3 * peer_grad16.astype(jnp.float32)
    mixed_numerators = 0.5 * (updated + peer_updated)
    mixed_weights = 0.5 * (push_weights + peer_weight)
    return (mixed_numerators[None], mixed_weights)


def solution(mesh):
    n_replica, n_fsdp = mesh.devices.shape
    split = Mesh(mesh.devices.reshape(n_replica, PAIR, n_fsdp // PAIR), ("replica", "fl", "fz"))
    rows = P("replica", ("fl", "fz"), None)
    return jax.shard_map(
        body,
        mesh=split,
        in_specs=(rows, P("replica"), P(), rows, rows, P()),
        out_specs=(rows, P("replica")),
        check_vma=False,
    )
```

```python
from functools import partial
import math

import jax
import jax.numpy as jnp
from jax import lax
from jax.sharding import Mesh, PartitionSpec as P

DIST_KINDS = 3
PAIR = 2


def passed_along(value, axis, steps):
    count = lax.axis_size(axis)
    pairs = [(source, (source + steps) % count) for source in range(count)]
    return lax.ppermute(value, axis, pairs)


def send_to_peer(pair, by):
    return passed_along(pair, "replica", by)


def to_peer(sender, operand, power):
    branches = [partial(sender, by=1 << bit) for bit in range(DIST_KINDS)]
    return lax.switch(power, branches, operand)


def body(numerators, push_weights, step_power, activations, targets, gain):
    numer = numerators[0]
    power = step_power[0]
    features = activations.shape[2]
    n_pair = lax.axis_size("fl")
    n_ring = lax.axis_size("fz")
    replica_tokens = activations.shape[1] * n_pair * n_ring
    params = (numer / push_weights[0]).astype(jnp.bfloat16)
    gathered = lax.all_gather(params, "fl", axis=0)
    gathered = lax.all_gather(gathered, "fz", axis=1)
    full_params = gathered.reshape(-1, params.shape[1])
    act32 = activations[0].astype(jnp.float32)
    mean_sq = jnp.mean(act32 * act32, axis=1, keepdims=True)
    scale = lax.rsqrt(mean_sq + 1e-05)
    normed = (act32 * scale * gain[None, :]).astype(jnp.bfloat16)
    tokens = normed.shape[0]
    side = lax.axis_index("fl")
    flip = [(i, n_pair - 1 - i) for i in range(n_pair)]
    row_width = features // n_pair
    own_cols = lax.dynamic_slice_in_dim(normed, side * row_width, row_width, axis=1)
    raw_partner = lax.dynamic_slice_in_dim(activations[0], (n_pair - 1 - side) * row_width, row_width, axis=1)
    their_raw = lax.ppermute(raw_partner, "fl", flip)
    their_scale = lax.ppermute(scale, "fl", flip)
    own_gain = lax.dynamic_slice_in_dim(gain, side * row_width, row_width)
    their_cols = (their_raw.astype(jnp.float32) * their_scale * own_gain[None, :]).astype(jnp.bfloat16)
    contract = (((0,), (0,)), ((), ()))
    half = tokens // 2
    mine = theirs = None
    for part in range(2):
        span = slice(part * half, (part + 1) * half)
        keys = jnp.dot(normed[span], full_params, preferred_element_type=jnp.float32) / math.sqrt(features)
        errors = ((keys - targets[0, span].astype(jnp.float32)) / math.sqrt(replica_tokens)).astype(
            jnp.bfloat16
        )
        their_errors = lax.ppermute(errors, "fl", flip)
        term = lax.dot_general(own_cols[span], errors, contract, preferred_element_type=jnp.float32)
        their_term = lax.dot_general(
            their_cols[span], their_errors, contract, preferred_element_type=jnp.float32
        )
        mine = term if mine is None else mine + term
        theirs = their_term if theirs is None else theirs + their_term
    pair_sum = mine.astype(jnp.bfloat16).astype(jnp.float32) + theirs.astype(jnp.bfloat16).astype(jnp.float32)
    blocks = pair_sum.astype(jnp.bfloat16).reshape(n_ring, -1, pair_sum.shape[1])
    early, weight, blocks = lax.optimization_barrier((numer, push_weights, blocks))
    peer_numer, peer_weight = to_peer(send_to_peer, (early, weight), power)
    grad16 = lax.psum_scatter(blocks, "fz", scatter_dimension=0)
    peer_grad16 = to_peer(send_to_peer, grad16, power)
    updated = numer - 0.3 * grad16.astype(jnp.float32)
    peer_updated = peer_numer - 0.3 * peer_grad16.astype(jnp.float32)
    mixed_numerators = 0.5 * (updated + peer_updated)
    mixed_weights = 0.5 * (push_weights + peer_weight)
    return (mixed_numerators[None], mixed_weights)


def solution(mesh):
    n_replica, n_fsdp = mesh.devices.shape
    split = Mesh(mesh.devices.reshape(n_replica, PAIR, n_fsdp // PAIR), ("replica", "fl", "fz"))
    rows = P("replica", ("fl", "fz"), None)
    return jax.shard_map(
        body,
        mesh=split,
        in_specs=(rows, P("replica"), P(), rows, rows, P()),
        out_specs=(rows, P("replica")),
        check_vma=False,
    )
```

```python
from functools import partial
import math

import jax
import jax.numpy as jnp
from jax import lax
from jax.sharding import Mesh, PartitionSpec as P

DIST_KINDS = 3
PAIR = 2


def passed_along(value, axis, steps):
    count = lax.axis_size(axis)
    pairs = [(source, (source + steps) % count) for source in range(count)]
    return lax.ppermute(value, axis, pairs)


def send_to_peer(pair, by):
    return passed_along(pair, "replica", by)


def to_peer(sender, operand, power):
    branches = [partial(sender, by=1 << bit) for bit in range(DIST_KINDS)]
    return lax.switch(power, branches, operand)


def body(numerators, push_weights, step_power, activations, targets, gain):
    numer = numerators[0]
    power = step_power[0]
    features = activations.shape[2]
    n_pair = lax.axis_size("fl")
    n_ring = lax.axis_size("fz")
    replica_tokens = activations.shape[1] * n_pair * n_ring
    params = (numer / push_weights[0]).astype(jnp.bfloat16)
    gathered = lax.all_gather(params, "fl", axis=0)
    gathered = lax.all_gather(gathered, "fz", axis=1)
    full_params = gathered.reshape(-1, params.shape[1])
    act32 = activations[0].astype(jnp.float32)
    mean_sq = jnp.mean(act32 * act32, axis=1, keepdims=True)
    normed = (act32 * lax.rsqrt(mean_sq + 1e-05) * gain[None, :]).astype(jnp.bfloat16)
    tokens = normed.shape[0]
    side = lax.axis_index("fl")
    flip = [(i, n_pair - 1 - i) for i in range(n_pair)]
    row_width = features // n_pair
    own_cols = lax.dynamic_slice_in_dim(normed, side * row_width, row_width, axis=1)
    partner_cols = lax.dynamic_slice_in_dim(normed, (n_pair - 1 - side) * row_width, row_width, axis=1)
    their_cols = lax.ppermute(partner_cols, "fl", flip)
    contract = (((0,), (0,)), ((), ()))
    half = tokens // 2
    mine = theirs = None
    for part in range(2):
        span = slice(part * half, (part + 1) * half)
        keys = jnp.dot(normed[span], full_params, preferred_element_type=jnp.float32) / math.sqrt(features)
        errors = ((keys - targets[0, span].astype(jnp.float32)) / math.sqrt(replica_tokens)).astype(
            jnp.bfloat16
        )
        their_errors = lax.ppermute(errors, "fl", flip)
        term = lax.dot_general(own_cols[span], errors, contract, preferred_element_type=jnp.float32)
        their_term = lax.dot_general(
            their_cols[span], their_errors, contract, preferred_element_type=jnp.float32
        )
        mine = term if mine is None else mine + term
        theirs = their_term if theirs is None else theirs + their_term
    pair_sum = mine.astype(jnp.bfloat16).astype(jnp.float32) + theirs.astype(jnp.bfloat16).astype(jnp.float32)
    blocks = pair_sum.astype(jnp.bfloat16).reshape(n_ring, -1, pair_sum.shape[1])
    early, weight, blocks = lax.optimization_barrier((numer, push_weights, blocks))
    peer_numer, peer_weight = to_peer(send_to_peer, (early, weight), power)
    grad16 = lax.psum_scatter(blocks, "fz", scatter_dimension=0)
    numer_mean, grad16 = lax.optimization_barrier((0.5 * (numer + peer_numer), grad16))
    peer_grad16 = to_peer(send_to_peer, grad16, power)
    mixed_numerators = numer_mean - 0.15 * (grad16.astype(jnp.float32) + peer_grad16.astype(jnp.float32))
    mixed_weights = 0.5 * (push_weights + peer_weight)
    return (mixed_numerators[None], mixed_weights)


def solution(mesh):
    n_replica, n_fsdp = mesh.devices.shape
    split = Mesh(mesh.devices.reshape(n_replica, PAIR, n_fsdp // PAIR), ("replica", "fl", "fz"))
    rows = P("replica", ("fl", "fz"), None)
    return jax.shard_map(
        body,
        mesh=split,
        in_specs=(rows, P("replica"), P(), rows, rows, P()),
        out_specs=(rows, P("replica")),
        check_vma=False,
    )
```

```python
from functools import partial
import math

import jax
import jax.numpy as jnp
from jax import lax
from jax.sharding import Mesh, PartitionSpec as P

DIST_KINDS = 3
PAIR = 2


def passed_along(value, axis, steps):
    count = lax.axis_size(axis)
    pairs = [(source, (source + steps) % count) for source in range(count)]
    return lax.ppermute(value, axis, pairs)


def send_to_peer(pair, by):
    return passed_along(pair, "replica", by)


def to_peer(sender, operand, power):
    branches = [partial(sender, by=1 << bit) for bit in range(DIST_KINDS)]
    return lax.switch(power, branches, operand)


def body(numerators, push_weights, step_power, activations, targets, gain):
    numer = numerators[0]
    power = step_power[0]
    features = activations.shape[2]
    n_pair = lax.axis_size("fl")
    n_ring = lax.axis_size("fz")
    replica_tokens = activations.shape[1] * n_pair * n_ring
    params = (numer / push_weights[0]).astype(jnp.bfloat16)
    gathered = lax.all_gather(params, "fl", axis=0)
    gathered = lax.all_gather(gathered, "fz", axis=1)
    full_params = gathered.reshape(-1, params.shape[1])
    act32 = activations[0].astype(jnp.float32)
    mean_sq = jnp.mean(act32 * act32, axis=1, keepdims=True)
    normed = (act32 * lax.rsqrt(mean_sq + 1e-05) * gain[None, :]).astype(jnp.bfloat16)
    tokens = normed.shape[0]
    side = lax.axis_index("fl")
    flip = [(i, n_pair - 1 - i) for i in range(n_pair)]
    row_width = features // n_pair
    own_cols = lax.dynamic_slice_in_dim(normed, side * row_width, row_width, axis=1)
    partner_cols = lax.dynamic_slice_in_dim(normed, (n_pair - 1 - side) * row_width, row_width, axis=1)
    their_cols = lax.ppermute(partner_cols, "fl", flip)
    contract = (((0,), (0,)), ((), ()))
    cut = tokens * 2 // 3
    mine = theirs = None
    for span in (slice(0, cut), slice(cut, tokens)):
        keys = jnp.dot(normed[span], full_params, preferred_element_type=jnp.float32) / math.sqrt(features)
        errors = ((keys - targets[0, span].astype(jnp.float32)) / math.sqrt(replica_tokens)).astype(
            jnp.bfloat16
        )
        their_errors = lax.ppermute(errors, "fl", flip)
        term = lax.dot_general(own_cols[span], errors, contract, preferred_element_type=jnp.float32)
        their_term = lax.dot_general(
            their_cols[span], their_errors, contract, preferred_element_type=jnp.float32
        )
        mine = term if mine is None else mine + term
        theirs = their_term if theirs is None else theirs + their_term
    pair_sum = mine.astype(jnp.bfloat16).astype(jnp.float32) + theirs.astype(jnp.bfloat16).astype(jnp.float32)
    blocks = pair_sum.astype(jnp.bfloat16).reshape(n_ring, -1, pair_sum.shape[1])
    early, weight, blocks = lax.optimization_barrier((numer, push_weights, blocks))
    peer_numer, peer_weight = to_peer(send_to_peer, (early, weight), power)
    grad16 = lax.psum_scatter(blocks, "fz", scatter_dimension=0)
    numer_mean, grad16 = lax.optimization_barrier((0.5 * (numer + peer_numer), grad16))
    peer_grad16 = to_peer(send_to_peer, grad16, power)
    mixed_numerators = numer_mean - 0.15 * (grad16.astype(jnp.float32) + peer_grad16.astype(jnp.float32))
    mixed_weights = 0.5 * (push_weights + peer_weight)
    return (mixed_numerators[None], mixed_weights)


def solution(mesh):
    n_replica, n_fsdp = mesh.devices.shape
    split = Mesh(mesh.devices.reshape(n_replica, PAIR, n_fsdp // PAIR), ("replica", "fl", "fz"))
    rows = P("replica", ("fl", "fz"), None)
    return jax.shard_map(
        body,
        mesh=split,
        in_specs=(rows, P("replica"), P(), rows, rows, P()),
        out_specs=(rows, P("replica")),
        check_vma=False,
    )
```
